128 devices in a mesh: ang: 64 (over x, y_lo, z, core), pix: 2 (over y_hi).
Axes of the slice: x: 4, y: 4 (y_hi: 2, y_lo: 2; y = y_hi * 2 + y_lo), z: 4, core: 2. Of those that a mesh axis runs over, the one named last changes fastest.
Arguments:
- grads: bfloat16 [2, 4096, 128, 512], P(None, 'ang', 'pix')
- circle_pos: int32 [4096], replicated, may hold values from 0 to 4095, as said below
- harmonics: int32 [256], replicated, may hold values from 0 to 4095, as said below
- support: int32 [128, 512], replicated, may hold values 0 or 1
Outputs:
- update: bfloat16 [2, 4096, 128, 512], P(None, 'ang', 'pix')
- harmonic_rms: float32 [256], replicated
The draws below stay inside these ranges and needn't reach their ends.
Inputs may be any that keep to these rules, and one draw needn't show every extreme that they name: `circle_pos`: the stored angles form 64 aligned blocks of 64 rows; block b holds the circle positions r_b + 64 * j for j = 0 to 63 in this order, and the 64 values r_b are distinct. `harmonics`: 256 distinct harmonic numbers, among them 0 and 4095.
All inputs are finite; a program needn't handle non-finite values.
Results may differ from the reference program's by a relative error of at most 0.015.
Values may be sent and summed in bfloat16 or wider, within the bound.
No kernel may reach another device: no remote copies, remote signals or barrier semaphores. Data moves between devices by JAX's collectives and lax.ppermute only.
A program may use at most 192 MiB of HBM per device.

```python
import math
import jax
import jax.numpy as jnp
from jax import lax

A1 = 64
A2 = 64
K = 256
W = 512
ROWS = 128


def circle_list(key):
    residues = jax.random.permutation(jax.random.fold_in(key, 7), A1).astype(jnp.int32)
    offsets = jnp.arange(A2, dtype=jnp.int32) * A1
    return (residues[:, None] + offsets[None, :]).reshape(-1)


def harmonic_order(key):
    return jax.random.permutation(jax.random.fold_in(key, 11), A1 * A2 - 2).astype(jnp.int32) + 1


def draw_circle_pos(key, part):
    return circle_list(key)


def draw_harmonics(key, part):
    inner = harmonic_order(key)[:K - 2]
    chosen = jnp.concatenate([jnp.array([0, A1 * A2 - 1], jnp.int32), inner])
    return jax.random.permutation(jax.random.fold_in(key, 23), chosen)


def draw_grads(key, part):
    subkeys = jax.random.split(jax.random.fold_in(key, 31), 5)
    cycle_total = A1 * A2
    row_ramp = 3.0 ** (jnp.arange(ROWS, dtype=jnp.float32) / (ROWS - 1))
    row_factor = jnp.exp(jax.random.uniform(subkeys[0], (ROWS,), jnp.float32, 0.0, math.log(3.3)))
    col_factor = jnp.exp(jax.random.uniform(subkeys[1], (W,), jnp.float32, 0.0, math.log(3.3)))
    pixel_scale = (row_ramp * row_factor)[:, None] * col_factor[None, :]
    full_shape = (2, cycle_total, ROWS, W)
    positions = circle_list(key)
    order = harmonic_order(key)
    chosen_harmonics = jnp.concatenate([order[K - 2:K], order[:4]])
    amplitudes = [0.8, 0.8, 0.04, 0.06, 0.08, 0.1]
    offsets = jax.random.uniform(subkeys[4], (6, ROWS, W), jnp.float32, -math.pi, math.pi)
    coherent_re = jnp.zeros((cycle_total, ROWS, W), jnp.float32)
    coherent_im = jnp.zeros((cycle_total, ROWS, W), jnp.float32)
    for term_index in range(6):
        turn_count = chosen_harmonics[term_index] * positions % cycle_total
        phase_angle = turn_count.astype(jnp.float32) * (2.0 * math.pi / cycle_total)
        circle_cos = jnp.cos(phase_angle)[:, None, None]
        circle_sin = jnp.sin(phase_angle)[:, None, None]
        pixel_cos = jnp.cos(offsets[term_index])[None]
        pixel_sin = jnp.sin(offsets[term_index])[None]
        coherent_re = coherent_re + amplitudes[term_index] * (circle_cos * pixel_cos - circle_sin * pixel_sin)
        coherent_im = coherent_im + amplitudes[term_index] * (circle_sin * pixel_cos + circle_cos * pixel_sin)
    coherent = jnp.stack((coherent_re, coherent_im))
    values = pixel_scale[None, None] * (jax.random.normal(subkeys[2], full_shape, jnp.float32) + coherent)
    return values.astype(jnp.bfloat16)


def touch_ends(result, stream_key, low, high):
    index_at = [jax.random.randint(jax.random.fold_in(stream_key, axis), (), 0, length) for axis, length in enumerate(result.shape)]
    widest = result.shape.index(max(result.shape))
    beside = index_at[:widest] + [(index_at[widest] + 1) % result.shape[widest]] + index_at[widest + 1:]
    return result.at[tuple(index_at)].set(low).at[tuple(beside)].set(high)


def setup_inputs(seed: int = 0) -> dict:
    streams_of = jax.random.split(jax.random.key(seed), 5)
    return {
        "grads": draw_grads(jax.random.fold_in(streams_of[4], 71), 0),
        "circle_pos": draw_circle_pos(jax.random.fold_in(streams_of[4], 71), 0),
        "harmonics": draw_harmonics(jax.random.fold_in(streams_of[4], 71), 0),
        "support": touch_ends((jax.random.randint(streams_of[3], (ROWS, W), 0, 4) < 3).astype(jnp.int32), jax.random.fold_in(streams_of[3], 1), 0, 1),
    }


def reference(grads, circle_pos, harmonics, support):
    angle_count = circle_pos.shape[0]
    kept_count = harmonics.shape[0]
    row_count = grads.shape[2]
    col_count = grads.shape[3]
    group_count = row_count // 8
    blocked = jnp.moveaxis(grads.reshape(2, angle_count, group_count, 8, col_count), 2, 0)

    def forward(portion):
        field = lax.complex(portion[0].astype(jnp.float32), portion[1].astype(jnp.float32))
        on_circle = jnp.zeros_like(field).at[circle_pos].set(field)
        spectrum = jnp.fft.fft(on_circle, axis=0)[harmonics] / jnp.sqrt(jnp.float32(angle_count))
        return jnp.stack((jnp.real(spectrum), jnp.imag(spectrum)))
    coefficients = lax.map(forward, blocked)
    weight = support.astype(jnp.float32).reshape(group_count, 1, 1, 8, col_count)
    square_sums = lax.optimization_barrier(jnp.sum(weight * coefficients * coefficients, axis=(0, 1, 3, 4)))
    harmonic_rms = jnp.sqrt(square_sums / (row_count * col_count) + 1e-06)
    step_field = weight * coefficients / harmonic_rms[None, None, :, None, None]

    def backward(portion):
        values = lax.complex(portion[0], portion[1])
        spectrum = jnp.zeros((angle_count,) + values.shape[1:], values.dtype).at[harmonics].set(values)
        on_circle = jnp.fft.ifft(spectrum, axis=0) * angle_count
        picked = on_circle[circle_pos] / jnp.sqrt(jnp.float32(kept_count))
        return jnp.stack((jnp.real(picked), jnp.imag(picked))).astype(jnp.bfloat16)
    update = lax.map(backward, step_field)
    update = jnp.moveaxis(update, 0, 2).reshape(2, angle_count, row_count, col_count)
    return (update, harmonic_rms)
```

```python
import math

import jax
import jax.numpy as jnp
from jax import lax
from jax.sharding import PartitionSpec as P


def phase_pair(product, modulus):
    radians = (product % modulus).astype(jnp.float32) * (2.0 * math.pi / modulus)
    return (jnp.cos(radians), jnp.sin(radians))


def split_parts(value):
    if value.dtype == jnp.bfloat16:
        return (value,)
    high = value.astype(jnp.bfloat16)
    low = (value - high.astype(jnp.float32)).astype(jnp.bfloat16)
    return (high, low)


def split_dot(left, right, dims):
    left_parts = split_parts(left)
    right_parts = split_parts(right)
    total = None
    for left_rank, left_piece in enumerate(left_parts):
        for right_rank, right_piece in enumerate(right_parts):
            if left_rank + right_rank <= 1:
                term = lax.dot_general(
                    left_piece, right_piece, (dims, ((), ())), preferred_element_type=jnp.float32
                )
                total = term if total is None else total + term
    return total


def global_sum(value):
    gathered = lax.all_gather(value, ("ang", "pix"))
    return jnp.sum(gathered, axis=0)


def body(grads, circle_pos, harmonics, support):
    ang_count = lax.axis_size("ang")
    _, block, row_pix, col_count = grads.shape
    angle_count = circle_pos.shape[0]
    kept_count = harmonics.shape[0]
    row_local = row_pix // ang_count
    row_start = lax.axis_index("pix") * row_pix + lax.axis_index("ang") * row_local
    weight = lax.dynamic_slice_in_dim(support, row_start, row_local, 0).astype(jnp.float32)
    weight = weight.reshape(-1)
    pixel_count = row_local * col_count
    cell_count = float(row_pix * lax.axis_size("pix") * col_count)

    send = jnp.transpose(grads, (2, 1, 0, 3)).reshape(row_pix, block, 2 * col_count)
    moved = lax.all_to_all(send, "ang", split_axis=0, concat_axis=0, tiled=True)
    flat = moved.reshape(ang_count, row_local, block, 2, col_count)
    flat = jnp.transpose(flat, (0, 2, 3, 1, 4)).reshape(angle_count, 2 * pixel_count)

    phase_cos, phase_sin = phase_pair(harmonics[:, None] * circle_pos[None, :], angle_count)
    table = jnp.concatenate((phase_cos, phase_sin), 0)
    products = split_dot(table, flat, ((1,), (0,)))
    scale = 1.0 / math.sqrt(angle_count)
    coef_re = (products[:kept_count, :pixel_count] + products[kept_count:, pixel_count:]) * scale
    coef_im = (products[:kept_count, pixel_count:] - products[kept_count:, :pixel_count]) * scale

    square_sums = jnp.sum(weight[None, :] * (coef_re * coef_re + coef_im * coef_im), axis=1)
    harmonic_rms = jnp.sqrt(global_sum(square_sums) / cell_count + 1e-06)
    factor = weight[None, :] / harmonic_rms[:, None]
    step_re = coef_re * factor
    step_im = coef_im * factor

    right_side = jnp.concatenate(
        (jnp.concatenate((step_re, step_im), 1), jnp.concatenate((-step_im, step_re), 1)), 0
    )
    synthesis = split_dot(table, right_side, ((0,), (0,)))
    scale_back = 1.0 / math.sqrt(kept_count)
    update = (synthesis * scale_back).astype(jnp.bfloat16)
    update = update.reshape(ang_count, block, 2, row_local, col_count)
    update = jnp.transpose(update, (0, 3, 1, 2, 4)).reshape(ang_count * row_local, block, 2 * col_count)
    back = lax.all_to_all(update, "ang", split_axis=0, concat_axis=0, tiled=True)
    back = jnp.transpose(back.reshape(row_pix, block, 2, col_count), (2, 1, 0, 3))
    return (back, harmonic_rms)


def solution(mesh):
    placed = (P(None, "ang", "pix", None), P(), P(), P())
    return jax.shard_map(
        body,
        mesh=mesh,
        in_specs=placed,
        out_specs=(P(None, "ang", "pix", None), P()),
        check_vma=False,
    )
```

```python
import math

import jax
import jax.numpy as jnp
from jax import lax
from jax.sharding import Mesh
from jax.sharding import PartitionSpec as P

ANG = ("x", "yl", "z", "c")
ALL = ANG + ("pix",)


def phase_pair(product, modulus):
    radians = (product % modulus).astype(jnp.float32) * (2.0 * math.pi / modulus)
    return (jnp.cos(radians), jnp.sin(radians))


def split_parts(value):
    if value.dtype == jnp.bfloat16:
        return (value,)
    high = value.astype(jnp.bfloat16)
    low = (value - high.astype(jnp.float32)).astype(jnp.bfloat16)
    return (high, low)


def split_dot(left, right, dims):
    left_parts = split_parts(left)
    right_parts = split_parts(right)
    total = None
    for left_rank, left_piece in enumerate(left_parts):
        for right_rank, right_piece in enumerate(right_parts):
            if left_rank + right_rank <= 1:
                term = lax.dot_general(
                    left_piece, right_piece, (dims, ((), ())), preferred_element_type=jnp.float32
                )
                total = term if total is None else total + term
    return total


def global_sum(value):
    for axis in ("c", "pix", "yl", "x", "z"):
        size = lax.axis_size(axis)
        shift = 1
        while shift < size:
            perm = [(i, (i + shift) % size) for i in range(size)]
            value = value + lax.ppermute(value, axis, perm)
            shift *= 2
    return value


def body(grads, circle_pos, harmonics, support):
    ang_count = lax.axis_size(ANG)
    _, block, row_pix, col_count = grads.shape
    angle_count = circle_pos.shape[0]
    kept_count = harmonics.shape[0]
    row_start = lax.axis_index("pix") * row_pix + lax.axis_index(ANG)
    weight = lax.dynamic_slice_in_dim(support, row_start, 1, 0).astype(jnp.float32).reshape(-1)
    cell_count = float(row_pix * lax.axis_size("pix") * col_count)

    send = jnp.transpose(grads, (2, 0, 1, 3))
    moved = lax.all_to_all(send, ANG, split_axis=0, concat_axis=0, tiled=True)
    flat = moved.reshape(ang_count * 2 * block, col_count)

    phase_cos, phase_sin = phase_pair(harmonics[:, None] * circle_pos[None, :], angle_count)
    phase_cos = phase_cos.reshape(kept_count, ang_count, 1, block)
    phase_sin = phase_sin.reshape(kept_count, ang_count, 1, block)
    table = jnp.concatenate(
        (
            jnp.concatenate((phase_cos, phase_sin), 2),
            jnp.concatenate((-phase_sin, phase_cos), 2),
        ),
        0,
    ).reshape(2 * kept_count, ang_count * 2 * block)

    coef = split_dot(table, flat, ((1,), (0,))) * (1.0 / math.sqrt(angle_count))
    coef_re = coef[:kept_count]
    coef_im = coef[kept_count:]
    square_sums = jnp.sum(weight[None, :] * (coef_re * coef_re + coef_im * coef_im), axis=1)
    harmonic_rms = jnp.sqrt(global_sum(square_sums) / cell_count + 1e-06)
    factor = weight[None, :] / harmonic_rms[:, None]
    step = coef * jnp.concatenate((factor, factor), 0)

    synthesis = split_dot(table, step, ((0,), (0,)))
    update = (synthesis * (1.0 / math.sqrt(kept_count))).astype(jnp.bfloat16)
    update = update.reshape(ang_count, 2, block, col_count)
    back = lax.all_to_all(update, ANG, split_axis=0, concat_axis=0, tiled=True)
    back = jnp.transpose(back, (1, 2, 0, 3))
    return (back, harmonic_rms)


def solution(mesh):
    devices = mesh.devices.reshape(4, 2, 4, 2, mesh.shape["pix"])
    physical = Mesh(devices, ALL)
    placed = (P(None, ANG, "pix", None), P(), P(), P())
    return jax.shard_map(
        body,
        mesh=physical,
        in_specs=placed,
        out_specs=(P(None, ANG, "pix", None), P()),
        check_vma=False,
    )
```

```python
import math

import jax
import jax.numpy as jnp
from jax import lax
from jax.sharding import Mesh
from jax.sharding import PartitionSpec as P

ANG = ("x", "yl", "z", "c")
ALL = ANG + ("pix",)


def phase_pair(product, modulus):
    radians = (product % modulus).astype(jnp.float32) * (2.0 * math.pi / modulus)
    return (jnp.cos(radians), jnp.sin(radians))


def split_parts(value):
    if value.dtype == jnp.bfloat16:
        return (value,)
    high = value.astype(jnp.bfloat16)
    low = (value - high.astype(jnp.float32)).astype(jnp.bfloat16)
    return (high, low)


def split_dot(left, right, dims):
    left_parts = split_parts(left)
    right_parts = split_parts(right)
    total = None
    for left_rank, left_piece in enumerate(left_parts):
        for right_rank, right_piece in enumerate(right_parts):
            if left_rank + right_rank <= 1:
                term = lax.dot_general(
                    left_piece, right_piece, (dims, ((), ())), preferred_element_type=jnp.float32
                )
                total = term if total is None else total + term
    return total


def global_sum(value):
    for axis in ("c", "pix", "yl", "x", "z"):
        size = lax.axis_size(axis)
        shift = 1
        while shift < size:
            perm = [(i, (i + shift) % size) for i in range(size)]
            value = value + lax.ppermute(value, axis, perm)
            shift *= 2
    return value


CHUNKS = 4


def phase_table(circle_pos, harmonics, ang_count, block):
    angle_count = circle_pos.shape[0]
    residues = circle_pos.reshape(ang_count, block)[:, 0]
    outer_cos, outer_sin = phase_pair(harmonics[:, None] * residues[None, :], angle_count)
    steps = jnp.arange(block, dtype=jnp.int32)
    inner_cos, inner_sin = phase_pair(harmonics[:, None] * steps[None, :], block)
    outer_cos = outer_cos[:, :, None]
    outer_sin = outer_sin[:, :, None]
    inner_cos = inner_cos[:, None, :]
    inner_sin = inner_sin[:, None, :]
    phase_cos = outer_cos * inner_cos - outer_sin * inner_sin
    phase_sin = outer_sin * inner_cos + outer_cos * inner_sin
    return (phase_cos, phase_sin)


def body(grads, circle_pos, harmonics, support):
    ang_count = lax.axis_size(ANG)
    _, block, row_pix, col_count = grads.shape
    angle_count = circle_pos.shape[0]
    kept_count = harmonics.shape[0]
    row_start = lax.axis_index("pix") * row_pix + lax.axis_index(ANG)
    weight = lax.dynamic_slice_in_dim(support, row_start, 1, 0).astype(jnp.float32).reshape(-1)
    cell_count = float(row_pix * lax.axis_size("pix") * col_count)
    width = block // CHUNKS

    phase_cos, phase_sin = phase_table(circle_pos, harmonics, ang_count, block)
    phase_cos = phase_cos[:, :, None, :]
    phase_sin = phase_sin[:, :, None, :]
    table = jnp.concatenate(
        (
            jnp.concatenate((phase_cos, phase_sin), 2),
            jnp.concatenate((-phase_sin, phase_cos), 2),
        ),
        0,
    )
    pieces = [
        table[:, :, :, c * width:(c + 1) * width].reshape(2 * kept_count, ang_count * 2 * width)
        for c in range(CHUNKS)
    ]

    coef = None
    for c in range(CHUNKS):
        send = jnp.transpose(grads[:, c * width:(c + 1) * width], (2, 0, 1, 3))
        moved = lax.all_to_all(send, ANG, split_axis=0, concat_axis=0, tiled=True)
        flat = moved.reshape(ang_count * 2 * width, col_count)
        part = split_dot(pieces[c], flat, ((1,), (0,)))
        coef = part if coef is None else coef + part
    coef = coef * (1.0 / math.sqrt(angle_count))
    coef_re = coef[:kept_count]
    coef_im = coef[kept_count:]
    square_sums = jnp.sum(weight[None, :] * (coef_re * coef_re + coef_im * coef_im), axis=1)
    harmonic_rms = jnp.sqrt(global_sum(square_sums) / cell_count + 1e-06)
    factor = weight[None, :] / harmonic_rms[:, None]
    step = coef * jnp.concatenate((factor, factor), 0)

    outs = []
    for c in range(CHUNKS):
        synthesis = split_dot(pieces[c], step, ((0,), (0,)))
        update = (synthesis * (1.0 / math.sqrt(kept_count))).astype(jnp.bfloat16)
        update = update.reshape(ang_count, 2, width, col_count)
        back = lax.all_to_all(update, ANG, split_axis=0, concat_axis=0, tiled=True)
        outs.append(jnp.transpose(back, (1, 2, 0, 3)))
    return (jnp.concatenate(outs, 1), harmonic_rms)


def solution(mesh):
    devices = mesh.devices.reshape(4, 2, 4, 2, mesh.shape["pix"])
    physical = Mesh(devices, ALL)
    placed = (P(None, ANG, "pix", None), P(), P(), P())
    return jax.shard_map(
        body,
        mesh=physical,
        in_specs=placed,
        out_specs=(P(None, ANG, "pix", None), P()),
        check_vma=False,
    )
```

```python
import math

import jax
import jax.numpy as jnp
from jax import lax
from jax.sharding import Mesh
from jax.sharding import PartitionSpec as P

ANG = ("x", "yl", "z", "c")
ALL = ANG + ("pix",)


def phase_pair(product, modulus):
    radians = (product % modulus).astype(jnp.float32) * (2.0 * math.pi / modulus)
    return (jnp.cos(radians), jnp.sin(radians))


def split_parts(value):
    if value.dtype == jnp.bfloat16:
        return (value,)
    high = value.astype(jnp.bfloat16)
    low = (value - high.astype(jnp.float32)).astype(jnp.bfloat16)
    return (high, low)


def split_dot(left, right, dims):
    left_parts = split_parts(left)
    right_parts = split_parts(right)
    total = None
    for left_rank, left_piece in enumerate(left_parts):
        for right_rank, right_piece in enumerate(right_parts):
            if left_rank + right_rank <= 1:
                term = lax.dot_general(
                    left_piece, right_piece, (dims, ((), ())), preferred_element_type=jnp.float32
                )
                total = term if total is None else total + term
    return total


def global_sum(value):
    for axis in ("c", "pix", "yl", "x", "z"):
        size = lax.axis_size(axis)
        shift = 1
        while shift < size:
            perm = [(i, (i + shift) % size) for i in range(size)]
            value = value + lax.ppermute(value, axis, perm)
            shift *= 2
    return value


def phase_table(circle_pos, harmonics, ang_count, block):
    angle_count = circle_pos.shape[0]
    residues = circle_pos.reshape(ang_count, block)[:, 0]
    outer = phase_pair(harmonics[:, None] * residues[None, :], angle_count)
    steps = jnp.arange(block, dtype=jnp.int32)
    inner = phase_pair(harmonics[:, None] * steps[None, :], block)
    return (outer, inner)


def real_table(outer, inner, transposed):
    outer_cos, outer_sin = outer
    inner_cos, inner_sin = inner
    if transposed:
        outer_cos, outer_sin = outer_cos.T[:, None, None, :], outer_sin.T[:, None, None, :]
        inner_cos, inner_sin = inner_cos.T[None, None, :, :], inner_sin.T[None, None, :, :]
        axis_ri, axis_k = 1, 3
    else:
        outer_cos, outer_sin = outer_cos[:, :, None, None], outer_sin[:, :, None, None]
        inner_cos, inner_sin = inner_cos[:, None, None, :], inner_sin[:, None, None, :]
        axis_ri, axis_k = 2, 0
    phase_cos = outer_cos * inner_cos - outer_sin * inner_sin
    phase_sin = outer_sin * inner_cos + outer_cos * inner_sin
    return jnp.concatenate(
        (
            jnp.concatenate((phase_cos, phase_sin), axis_ri),
            jnp.concatenate((-phase_sin, phase_cos), axis_ri),
        ),
        axis_k,
    )


def body(grads, circle_pos, harmonics, support):
    ang_count = lax.axis_size(ANG)
    _, block, row_pix, col_count = grads.shape
    angle_count = circle_pos.shape[0]
    kept_count = harmonics.shape[0]
    row_start = lax.axis_index("pix") * row_pix + lax.axis_index(ANG)
    weight = lax.dynamic_slice_in_dim(support, row_start, 1, 0).astype(jnp.float32).reshape(-1)
    cell_count = float(row_pix * lax.axis_size("pix") * col_count)
    depth = ang_count * 2 * block

    send = jnp.transpose(grads, (2, 0, 1, 3))
    moved = lax.all_to_all(send, ANG, split_axis=0, concat_axis=0, tiled=True)
    flat = moved.reshape(depth, col_count)

    outer, inner = phase_table(circle_pos, harmonics, ang_count, block)
    forward_parts = split_parts(real_table(outer, inner, False).reshape(2 * kept_count, depth))
    backward_parts = split_parts(real_table(outer, inner, True).reshape(depth, 2 * kept_count))
    forward_parts, backward_parts = lax.optimization_barrier((forward_parts, backward_parts))

    coef = None
    for piece in forward_parts:
        term = jnp.dot(piece, flat, preferred_element_type=jnp.float32)
        coef = term if coef is None else coef + term
    coef = coef * (1.0 / math.sqrt(angle_count))
    coef_re = coef[:kept_count]
    coef_im = coef[kept_count:]
    square_sums = jnp.sum(weight[None, :] * (coef_re * coef_re + coef_im * coef_im), axis=1)
    harmonic_rms = jnp.sqrt(global_sum(square_sums) / cell_count + 1e-06)
    factor = weight[None, :] / harmonic_rms[:, None]
    step = coef * jnp.concatenate((factor, factor), 0)

    step_parts = split_parts(step)
    synthesis = None
    for left_rank, left_piece in enumerate(backward_parts):
        for right_rank, right_piece in enumerate(step_parts):
            if left_rank + right_rank <= 1:
                term = jnp.dot(left_piece, right_piece, preferred_element_type=jnp.float32)
                synthesis = term if synthesis is None else synthesis + term
    update = (synthesis * (1.0 / math.sqrt(kept_count))).astype(jnp.bfloat16)
    update = update.reshape(ang_count, 2, block, col_count)
    back = lax.all_to_all(update, ANG, split_axis=0, concat_axis=0, tiled=True)
    back = jnp.transpose(back, (1, 2, 0, 3))
    return (back, harmonic_rms)


def solution(mesh):
    devices = mesh.devices.reshape(4, 2, 4, 2, mesh.shape["pix"])
    physical = Mesh(devices, ALL)
    placed = (P(None, ANG, "pix", None), P(), P(), P())
    return jax.shard_map(
        body,
        mesh=physical,
        in_specs=placed,
        out_specs=(P(None, ANG, "pix", None), P()),
        check_vma=False,
    )
```

```python
import math

import jax
import jax.numpy as jnp
from jax import lax
from jax.sharding import Mesh
from jax.sharding import PartitionSpec as P

ANG = ("x", "yl", "z", "c")
ALL = ANG + ("pix",)


def phase_pair(product, modulus):
    radians = (product % modulus).astype(jnp.float32) * (2.0 * math.pi / modulus)
    return (jnp.cos(radians), jnp.sin(radians))


def split_parts(value):
    if value.dtype == jnp.bfloat16:
        return (value,)
    high = value.astype(jnp.bfloat16)
    low = (value - high.astype(jnp.float32)).astype(jnp.bfloat16)
    return (high, low)


def split_dot(left, right, dims):
    left_parts = split_parts(left)
    right_parts = split_parts(right)
    total = None
    for left_rank, left_piece in enumerate(left_parts):
        for right_rank, right_piece in enumerate(right_parts):
            if left_rank + right_rank <= 1:
                term = lax.dot_general(
                    left_piece, right_piece, (dims, ((), ())), preferred_element_type=jnp.float32
                )
                total = term if total is None else total + term
    return total


def global_sum(value):
    for axis in ("c", "pix", "yl", "x", "z"):
        size = lax.axis_size(axis)
        shift = 1
        while shift < size:
            perm = [(i, (i + shift) % size) for i in range(size)]
            value = value + lax.ppermute(value, axis, perm)
            shift *= 2
    return value


def phase_table(circle_pos, harmonics, ang_count, block):
    angle_count = circle_pos.shape[0]
    residues = circle_pos.reshape(ang_count, block)[:, 0]
    outer = phase_pair(harmonics[:, None] * residues[None, :], angle_count)
    steps = jnp.arange(block, dtype=jnp.int32)
    inner = phase_pair(harmonics[:, None] * steps[None, :], block)
    return (outer, inner)


def real_table(outer, inner, transposed):
    outer_cos, outer_sin = outer
    inner_cos, inner_sin = inner
    if transposed:
        outer_cos, outer_sin = outer_cos.T[:, None, None, :], outer_sin.T[:, None, None, :]
        inner_cos, inner_sin = inner_cos.T[None, None, :, :], inner_sin.T[None, None, :, :]
        axis_ri, axis_k = 1, 3
    else:
        outer_cos, outer_sin = outer_cos[:, :, None, None], outer_sin[:, :, None, None]
        inner_cos, inner_sin = inner_cos[:, None, None, :], inner_sin[:, None, None, :]
        axis_ri, axis_k = 2, 0
    phase_cos = outer_cos * inner_cos - outer_sin * inner_sin
    phase_sin = outer_sin * inner_cos + outer_cos * inner_sin
    return jnp.concatenate(
        (
            jnp.concatenate((phase_cos, phase_sin), axis_ri),
            jnp.concatenate((-phase_sin, phase_cos), axis_ri),
        ),
        axis_k,
    )


def body(grads, circle_pos, harmonics, support):
    ang_count = lax.axis_size(ANG)
    _, block, row_pix, col_count = grads.shape
    angle_count = circle_pos.shape[0]
    kept_count = harmonics.shape[0]
    row_start = lax.axis_index("pix") * row_pix + lax.axis_index(ANG)
    weight = lax.dynamic_slice_in_dim(support, row_start, 1, 0).astype(jnp.float32).reshape(-1)
    cell_count = float(row_pix * lax.axis_size("pix") * col_count)
    depth = ang_count * 2 * block

    send = jnp.transpose(grads, (2, 0, 1, 3))
    moved = lax.all_to_all(send, ANG, split_axis=0, concat_axis=0, tiled=True)
    flat = moved.reshape(depth, col_count)

    outer, inner = phase_table(circle_pos, harmonics, ang_count, block)
    forward_high, forward_low = split_parts(real_table(outer, inner, False).reshape(2 * kept_count, depth))
    backward_high, backward_low = split_parts(real_table(outer, inner, True).reshape(depth, 2 * kept_count))
    forward_table = jnp.concatenate((forward_high, forward_low), 0)
    backward_table = jnp.concatenate((backward_high, backward_low, backward_high), 1)
    forward_table, backward_table = lax.optimization_barrier((forward_table, backward_table))

    stacked = jnp.dot(forward_table, flat, preferred_element_type=jnp.float32)
    coef = (stacked[: 2 * kept_count] + stacked[2 * kept_count:]) * (1.0 / math.sqrt(angle_count))
    coef_re = coef[:kept_count]
    coef_im = coef[kept_count:]
    square_sums = jnp.sum(weight[None, :] * (coef_re * coef_re + coef_im * coef_im), axis=1)
    harmonic_rms = jnp.sqrt(global_sum(square_sums) / cell_count + 1e-06)
    factor = weight[None, :] / harmonic_rms[:, None]
    step = coef * jnp.concatenate((factor, factor), 0)

    step_high, step_low = split_parts(step)
    step_stack = jnp.concatenate((step_high, step_high, step_low), 0)
    synthesis = jnp.dot(backward_table, step_stack, preferred_element_type=jnp.float32)
    update = (synthesis * (1.0 / math.sqrt(kept_count))).astype(jnp.bfloat16)
    update = update.reshape(ang_count, 2, block, col_count)
    back = lax.all_to_all(update, ANG, split_axis=0, concat_axis=0, tiled=True)
    back = jnp.transpose(back, (1, 2, 0, 3))
    return (back, harmonic_rms)


def solution(mesh):
    devices = mesh.devices.reshape(4, 2, 4, 2, mesh.shape["pix"])
    physical = Mesh(devices, ALL)
    placed = (P(None, ANG, "pix", None), P(), P(), P())
    return jax.shard_map(
        body,
        mesh=physical,
        in_specs=placed,
        out_specs=(P(None, ANG, "pix", None), P()),
        check_vma=False,
    )
```

```python
import math

import jax
import jax.numpy as jnp
from jax import lax
from jax.sharding import Mesh
from jax.sharding import PartitionSpec as P

ANG = ("x", "yl", "z", "c")
ALL = ANG + ("pix",)


def phase_pair(product, modulus):
    radians = (product % modulus).astype(jnp.float32) * (2.0 * math.pi / modulus)
    return (jnp.cos(radians), jnp.sin(radians))


def split_parts(value):
    if value.dtype == jnp.bfloat16:
        return (value,)
    high = value.astype(jnp.bfloat16)
    low = (value - high.astype(jnp.float32)).astype(jnp.bfloat16)
    return (high, low)


def split_dot(left, right, dims):
    left_parts = split_parts(left)
    right_parts = split_parts(right)
    total = None
    for left_rank, left_piece in enumerate(left_parts):
        for right_rank, right_piece in enumerate(right_parts):
            if left_rank + right_rank <= 1:
                term = lax.dot_general(
                    left_piece, right_piece, (dims, ((), ())), preferred_element_type=jnp.float32
                )
                total = term if total is None else total + term
    return total


def global_sum(value):
    for axis in ("c", "pix", "yl", "x", "z"):
        size = lax.axis_size(axis)
        shift = 1
        while shift < size:
            perm = [(i, (i + shift) % size) for i in range(size)]
            value = value + lax.ppermute(value, axis, perm)
            shift *= 2
    return value


HALVES = 2


def phase_table(circle_pos, harmonics, ang_count, block):
    angle_count = circle_pos.shape[0]
    residues = circle_pos.reshape(ang_count, block)[:, 0]
    outer = phase_pair(harmonics[:, None] * residues[None, :], angle_count)
    steps = jnp.arange(block, dtype=jnp.int32)
    inner = phase_pair(harmonics[:, None] * steps[None, :], block)
    return (outer, inner)


def real_table(outer, inner, transposed):
    outer_cos, outer_sin = outer
    inner_cos, inner_sin = inner
    if transposed:
        outer_cos, outer_sin = outer_cos.T[:, None, None, :], outer_sin.T[:, None, None, :]
        inner_cos, inner_sin = inner_cos.T[None, None, :, :], inner_sin.T[None, None, :, :]
        axis_ri, axis_k = 1, 3
    else:
        outer_cos, outer_sin = outer_cos[:, :, None, None], outer_sin[:, :, None, None]
        inner_cos, inner_sin = inner_cos[:, None, None, :], inner_sin[:, None, None, :]
        axis_ri, axis_k = 2, 0
    phase_cos = outer_cos * inner_cos - outer_sin * inner_sin
    phase_sin = outer_sin * inner_cos + outer_cos * inner_sin
    return jnp.concatenate(
        (
            jnp.concatenate((phase_cos, phase_sin), axis_ri),
            jnp.concatenate((-phase_sin, phase_cos), axis_ri),
        ),
        axis_k,
    )


def body(grads, circle_pos, harmonics, support):
    ang_count = lax.axis_size(ANG)
    _, block, row_pix, col_count = grads.shape
    angle_count = circle_pos.shape[0]
    kept_count = harmonics.shape[0]
    row_start = lax.axis_index("pix") * row_pix + lax.axis_index(ANG)
    weight = lax.dynamic_slice_in_dim(support, row_start, 1, 0).astype(jnp.float32).reshape(-1)
    cell_count = float(row_pix * lax.axis_size("pix") * col_count)
    depth = ang_count * 2 * block

    half = col_count // HALVES
    outer, inner = phase_table(circle_pos, harmonics, ang_count, block)
    forward_high, forward_low = split_parts(real_table(outer, inner, False).reshape(2 * kept_count, depth))
    backward_high, backward_low = split_parts(real_table(outer, inner, True).reshape(depth, 2 * kept_count))
    forward_table = jnp.concatenate((forward_high, forward_low), 0)
    backward_table = jnp.concatenate((backward_high, backward_low, backward_high), 1)
    forward_table, backward_table = lax.optimization_barrier((forward_table, backward_table))

    coefs = []
    for h in range(HALVES):
        send = jnp.transpose(grads[:, :, :, h * half:(h + 1) * half], (2, 0, 1, 3))
        moved = lax.all_to_all(send, ANG, split_axis=0, concat_axis=0, tiled=True)
        stacked = jnp.dot(forward_table, moved.reshape(depth, half), preferred_element_type=jnp.float32)
        coefs.append((stacked[: 2 * kept_count] + stacked[2 * kept_count:]) * (1.0 / math.sqrt(angle_count)))
    coef = jnp.concatenate(coefs, 1)
    coef_re = coef[:kept_count]
    coef_im = coef[kept_count:]
    square_sums = jnp.sum(weight[None, :] * (coef_re * coef_re + coef_im * coef_im), axis=1)
    harmonic_rms = jnp.sqrt(global_sum(square_sums) / cell_count + 1e-06)
    factor = weight[None, :] / harmonic_rms[:, None]
    step = coef * jnp.concatenate((factor, factor), 0)

    step_high, step_low = split_parts(step)
    step_stack = jnp.concatenate((step_high, step_high, step_low), 0)
    synthesis = jnp.dot(backward_table, step_stack, preferred_element_type=jnp.float32)
    update = (synthesis * (1.0 / math.sqrt(kept_count))).astype(jnp.bfloat16)
    update = update.reshape(ang_count, 2, block, col_count)
    back = lax.all_to_all(update, ANG, split_axis=0, concat_axis=0, tiled=True)
    back = jnp.transpose(back, (1, 2, 0, 3))
    return (back, harmonic_rms)


def solution(mesh):
    devices = mesh.devices.reshape(4, 2, 4, 2, mesh.shape["pix"])
    physical = Mesh(devices, ALL)
    placed = (P(None, ANG, "pix", None), P(), P(), P())
    return jax.shard_map(
        body,
        mesh=physical,
        in_specs=placed,
        out_specs=(P(None, ANG, "pix", None), P()),
        check_vma=False,
    )
```

```python
import math

import jax
import jax.numpy as jnp
from jax import lax
from jax.sharding import Mesh
from jax.sharding import PartitionSpec as P

ANG = ("x", "yl", "z", "c")
ALL = ANG + ("pix",)


def phase_pair(product, modulus):
    radians = (product % modulus).astype(jnp.float32) * (2.0 * math.pi / modulus)
    return (jnp.cos(radians), jnp.sin(radians))


def split_parts(value):
    if value.dtype == jnp.bfloat16:
        return (value,)
    high = value.astype(jnp.bfloat16)
    low = (value - high.astype(jnp.float32)).astype(jnp.bfloat16)
    return (high, low)


def split_dot(left, right, dims):
    left_parts = split_parts(left)
    right_parts = split_parts(right)
    total = None
    for left_rank, left_piece in enumerate(left_parts):
        for right_rank, right_piece in enumerate(right_parts):
            if left_rank + right_rank <= 1:
                term = lax.dot_general(
                    left_piece, right_piece, (dims, ((), ())), preferred_element_type=jnp.float32
                )
                total = term if total is None else total + term
    return total


def global_sum(value):
    for axis in ("c", "pix", "yl", "x", "z"):
        size = lax.axis_size(axis)
        shift = 1
        while shift < size:
            perm = [(i, (i + shift) % size) for i in range(size)]
            value = value + lax.ppermute(value, axis, perm)
            shift *= 2
    return value


HALVES = 2


def phase_table(circle_pos, harmonics, ang_count, block):
    angle_count = circle_pos.shape[0]
    residues = circle_pos.reshape(ang_count, block)[:, 0]
    outer = phase_pair(harmonics[:, None] * residues[None, :], angle_count)
    steps = jnp.arange(block, dtype=jnp.int32)
    inner = phase_pair(harmonics[:, None] * steps[None, :], block)
    return (outer, inner)


def real_table(outer, inner, transposed):
    outer_cos, outer_sin = outer
    inner_cos, inner_sin = inner
    if transposed:
        outer_cos, outer_sin = outer_cos.T[:, None, None, :], outer_sin.T[:, None, None, :]
        inner_cos, inner_sin = inner_cos.T[None, None, :, :], inner_sin.T[None, None, :, :]
        axis_ri, axis_k = 1, 3
    else:
        outer_cos, outer_sin = outer_cos[:, :, None, None], outer_sin[:, :, None, None]
        inner_cos, inner_sin = inner_cos[:, None, None, :], inner_sin[:, None, None, :]
        axis_ri, axis_k = 2, 0
    phase_cos = outer_cos * inner_cos - outer_sin * inner_sin
    phase_sin = outer_sin * inner_cos + outer_cos * inner_sin
    return jnp.concatenate(
        (
            jnp.concatenate((phase_cos, phase_sin), axis_ri),
            jnp.concatenate((-phase_sin, phase_cos), axis_ri),
        ),
        axis_k,
    )


def body(grads, circle_pos, harmonics, support):
    ang_count = lax.axis_size(ANG)
    _, block, row_pix, col_count = grads.shape
    angle_count = circle_pos.shape[0]
    kept_count = harmonics.shape[0]
    row_start = lax.axis_index("pix") * row_pix + lax.axis_index(ANG)
    weight = lax.dynamic_slice_in_dim(support, row_start, 1, 0).astype(jnp.float32).reshape(-1)
    cell_count = float(row_pix * lax.axis_size("pix") * col_count)
    depth = ang_count * 2 * block

    half = col_count // HALVES
    outer, inner = phase_table(circle_pos, harmonics, ang_count, block)
    forward_high, forward_low = split_parts(real_table(outer, inner, False).reshape(2 * kept_count, depth))
    forward_table = lax.optimization_barrier(jnp.concatenate((forward_high, forward_low), 0))

    coefs = []
    for h in range(HALVES):
        send = jnp.transpose(grads[:, :, :, h * half:(h + 1) * half], (2, 0, 1, 3))
        moved = lax.all_to_all(send, ANG, split_axis=0, concat_axis=0, tiled=True)
        if h == 1:
            moved, backward_table = lax.optimization_barrier((moved, backward_table))
        stacked = jnp.dot(forward_table, moved.reshape(depth, half), preferred_element_type=jnp.float32)
        if h == 0:
            outer, inner, stacked = lax.optimization_barrier((outer, inner, stacked))
            backward_high, backward_low = split_parts(
                real_table(outer, inner, True).reshape(depth, 2 * kept_count)
            )
            backward_table = jnp.concatenate((backward_high, backward_low, backward_high), 1)
        coefs.append((stacked[: 2 * kept_count] + stacked[2 * kept_count:]) * (1.0 / math.sqrt(angle_count)))
    coef = jnp.concatenate(coefs, 1)
    coef_re = coef[:kept_count]
    coef_im = coef[kept_count:]
    square_sums = jnp.sum(weight[None, :] * (coef_re * coef_re + coef_im * coef_im), axis=1)
    harmonic_rms = jnp.sqrt(global_sum(square_sums) / cell_count + 1e-06)
    factor = weight[None, :] / harmonic_rms[:, None]
    step = coef * jnp.concatenate((factor, factor), 0)

    step_high, step_low = split_parts(step)
    step_stack = jnp.concatenate((step_high, step_high, step_low), 0)
    synthesis = jnp.dot(backward_table, step_stack, preferred_element_type=jnp.float32)
    update = (synthesis * (1.0 / math.sqrt(kept_count))).astype(jnp.bfloat16)
    update = update.reshape(ang_count, 2, block, col_count)
    back = lax.all_to_all(update, ANG, split_axis=0, concat_axis=0, tiled=True)
    back = jnp.transpose(back, (1, 2, 0, 3))
    return (back, harmonic_rms)


def solution(mesh):
    devices = mesh.devices.reshape(4, 2, 4, 2, mesh.shape["pix"])
    physical = Mesh(devices, ALL)
    placed = (P(None, ANG, "pix", None), P(), P(), P())
    return jax.shard_map(
        body,
        mesh=physical,
        in_specs=placed,
        out_specs=(P(None, ANG, "pix", None), P()),
        check_vma=False,
    )
```

```python
import math

import jax
import jax.numpy as jnp
from jax import lax
from jax.experimental.layout import Layout, with_layout_constraint
from jax.sharding import Mesh
from jax.sharding import PartitionSpec as P

ANG = ("x", "yl", "z", "c")
ALL = ANG + ("pix",)


def phase_pair(product, modulus):
    radians = (product % modulus).astype(jnp.float32) * (2.0 * math.pi / modulus)
    return (jnp.cos(radians), jnp.sin(radians))


def split_parts(value):
    if value.dtype == jnp.bfloat16:
        return (value,)
    high = value.astype(jnp.bfloat16)
    low = (value - high.astype(jnp.float32)).astype(jnp.bfloat16)
    return (high, low)


def split_dot(left, right, dims):
    left_parts = split_parts(left)
    right_parts = split_parts(right)
    total = None
    for left_rank, left_piece in enumerate(left_parts):
        for right_rank, right_piece in enumerate(right_parts):
            if left_rank + right_rank <= 1:
                term = lax.dot_general(
                    left_piece, right_piece, (dims, ((), ())), preferred_element_type=jnp.float32
                )
                total = term if total is None else total + term
    return total


def global_sum(value):
    for axis in ("c", "pix", "yl", "x", "z"):
        size = lax.axis_size(axis)
        shift = 1
        while shift < size:
            perm = [(i, (i + shift) % size) for i in range(size)]
            value = value + lax.ppermute(value, axis, perm)
            shift *= 2
    return value


HALVES = 2


def phase_table(circle_pos, harmonics, ang_count, block):
    angle_count = circle_pos.shape[0]
    residues = circle_pos.reshape(ang_count, block)[:, 0]
    outer = phase_pair(harmonics[:, None] * residues[None, :], angle_count)
    steps = jnp.arange(block, dtype=jnp.int32)
    inner = phase_pair(harmonics[:, None] * steps[None, :], block)
    return (outer, inner)


def real_table(outer, inner, transposed):
    outer_cos, outer_sin = outer
    inner_cos, inner_sin = inner
    if transposed:
        outer_cos, outer_sin = outer_cos.T[:, None, None, :], outer_sin.T[:, None, None, :]
        inner_cos, inner_sin = inner_cos.T[None, None, :, :], inner_sin.T[None, None, :, :]
        axis_ri, axis_k = 1, 3
    else:
        outer_cos, outer_sin = outer_cos[:, :, None, None], outer_sin[:, :, None, None]
        inner_cos, inner_sin = inner_cos[:, None, None, :], inner_sin[:, None, None, :]
        axis_ri, axis_k = 2, 0
    phase_cos = outer_cos * inner_cos - outer_sin * inner_sin
    phase_sin = outer_sin * inner_cos + outer_cos * inner_sin
    return jnp.concatenate(
        (
            jnp.concatenate((phase_cos, phase_sin), axis_ri),
            jnp.concatenate((-phase_sin, phase_cos), axis_ri),
        ),
        axis_k,
    )


def body(grads, circle_pos, harmonics, support):
    ang_count = lax.axis_size(ANG)
    _, block, row_pix, col_count = grads.shape
    angle_count = circle_pos.shape[0]
    kept_count = harmonics.shape[0]
    row_start = lax.axis_index("pix") * row_pix + lax.axis_index(ANG)
    weight = lax.dynamic_slice_in_dim(support, row_start, 1, 0).astype(jnp.float32).reshape(-1)
    cell_count = float(row_pix * lax.axis_size("pix") * col_count)
    depth = ang_count * 2 * block

    half = col_count // HALVES
    width = block // HALVES
    outer, inner = phase_table(circle_pos, harmonics, ang_count, block)
    forward_high, forward_low = split_parts(real_table(outer, inner, False).reshape(2 * kept_count, depth))
    forward_table = lax.optimization_barrier(jnp.concatenate((forward_high, forward_low), 0))

    coefs = []
    for h in range(HALVES):
        send = jnp.transpose(grads[:, :, :, h * half:(h + 1) * half], (2, 0, 1, 3))
        moved = lax.all_to_all(send, ANG, split_axis=0, concat_axis=0, tiled=True)
        if h == 1:
            moved, backward_table = lax.optimization_barrier((moved, backward_table))
        stacked = jnp.dot(forward_table, moved.reshape(depth, half), preferred_element_type=jnp.float32)
        if h == 0:
            outer, inner, stacked = lax.optimization_barrier((outer, inner, stacked))
            backward_table = []
            for g in range(HALVES):
                part_inner = tuple(x[:, g * width:(g + 1) * width] for x in inner)
                backward_high, backward_low = split_parts(
                    real_table(outer, part_inner, True).reshape(depth // HALVES, 2 * kept_count)
                )
                backward_table.append(jnp.concatenate((backward_high, backward_low, backward_high), 1))
            backward_table = tuple(backward_table)
        coefs.append((stacked[: 2 * kept_count] + stacked[2 * kept_count:]) * (1.0 / math.sqrt(angle_count)))
    coef = jnp.concatenate(coefs, 1)
    coef_re = coef[:kept_count]
    coef_im = coef[kept_count:]
    square_sums = jnp.sum(weight[None, :] * (coef_re * coef_re + coef_im * coef_im), axis=1)
    harmonic_rms = jnp.sqrt(global_sum(square_sums) / cell_count + 1e-06)
    factor = weight[None, :] / harmonic_rms[:, None]
    step = coef * jnp.concatenate((factor, factor), 0)

    step_high, step_low = split_parts(step)
    step_stack = jnp.concatenate((step_high, step_high, step_low), 0)
    outs = []
    for g in range(HALVES):
        synthesis = jnp.dot(backward_table[g], step_stack, preferred_element_type=jnp.float32)
        update = (synthesis * (1.0 / math.sqrt(kept_count))).astype(jnp.bfloat16)
        update = update.reshape(ang_count, 2, width, col_count)
        back = lax.all_to_all(update, ANG, split_axis=0, concat_axis=0, tiled=True)
        back = jnp.transpose(back, (1, 2, 0, 3))
        outs.append(with_layout_constraint(back, Layout(major_to_minor=(0, 1, 2, 3))))
    back = jnp.concatenate(outs, 1)
    return (back, harmonic_rms)


def solution(mesh):
    devices = mesh.devices.reshape(4, 2, 4, 2, mesh.shape["pix"])
    physical = Mesh(devices, ALL)
    placed = (P(None, ANG, "pix", None), P(), P(), P())
    return jax.shard_map(
        body,
        mesh=physical,
        in_specs=placed,
        out_specs=(P(None, ANG, "pix", None), P()),
        check_vma=False,
    )
```

```python
import math

import jax
import jax.numpy as jnp
from jax import lax
from jax.sharding import Mesh
from jax.sharding import PartitionSpec as P

ANG = ("x", "yl", "z", "c")
ALL = ANG + ("pix",)


def phase_pair(product, modulus):
    radians = (product % modulus).astype(jnp.float32) * (2.0 * math.pi / modulus)
    return (jnp.cos(radians), jnp.sin(radians))


def split_parts(value):
    if value.dtype == jnp.bfloat16:
        return (value,)
    high = value.astype(jnp.bfloat16)
    low = (value - high.astype(jnp.float32)).astype(jnp.bfloat16)
    return (high, low)


def split_dot(left, right, dims):
    left_parts = split_parts(left)
    right_parts = split_parts(right)
    total = None
    for left_rank, left_piece in enumerate(left_parts):
        for right_rank, right_piece in enumerate(right_parts):
            if left_rank + right_rank <= 1:
                term = lax.dot_general(
                    left_piece, right_piece, (dims, ((), ())), preferred_element_type=jnp.float32
                )
                total = term if total is None else total + term
    return total


def global_sum(value):
    for axis in ("c", "pix", "yl", "x", "z"):
        size = lax.axis_size(axis)
        if size == 2:
            value = value + lax.ppermute(value, axis, [(0, 1), (1, 0)])
            continue
        parts = [value] + [
            lax.ppermute(value, axis, [(i, (i + shift) % size) for i in range(size)]) for shift in range(1, size)
        ]
        order = (lax.axis_index(axis) - jnp.arange(size)) % size
        ordered = jnp.stack(parts)[order]
        value = ordered[0]
        for position in range(1, size):
            value = value + ordered[position]
    return value


HALVES = 2


def phase_table(circle_pos, harmonics, ang_count, block):
    angle_count = circle_pos.shape[0]
    residues = circle_pos.reshape(ang_count, block)[:, 0]
    outer = phase_pair(harmonics[:, None] * residues[None, :], angle_count)
    steps = jnp.arange(block, dtype=jnp.int32)
    inner = phase_pair(harmonics[:, None] * steps[None, :], block)
    return (outer, inner)


def real_table(outer, inner, transposed):
    outer_cos, outer_sin = outer
    inner_cos, inner_sin = inner
    if transposed:
        outer_cos, outer_sin = outer_cos.T[:, None, None, :], outer_sin.T[:, None, None, :]
        inner_cos, inner_sin = inner_cos.T[None, None, :, :], inner_sin.T[None, None, :, :]
        axis_ri, axis_k = 1, 3
    else:
        outer_cos, outer_sin = outer_cos[:, :, None, None], outer_sin[:, :, None, None]
        inner_cos, inner_sin = inner_cos[:, None, None, :], inner_sin[:, None, None, :]
        axis_ri, axis_k = 2, 0
    phase_cos = outer_cos * inner_cos - outer_sin * inner_sin
    phase_sin = outer_sin * inner_cos + outer_cos * inner_sin
    return jnp.concatenate(
        (
            jnp.concatenate((phase_cos, phase_sin), axis_ri),
            jnp.concatenate((-phase_sin, phase_cos), axis_ri),
        ),
        axis_k,
    )


def body(grads, circle_pos, harmonics, support):
    ang_count = lax.axis_size(ANG)
    _, block, row_pix, col_count = grads.shape
    angle_count = circle_pos.shape[0]
    kept_count = harmonics.shape[0]
    row_start = lax.axis_index("pix") * row_pix + lax.axis_index(ANG)
    weight = lax.dynamic_slice_in_dim(support, row_start, 1, 0).astype(jnp.float32).reshape(-1)
    cell_count = float(row_pix * lax.axis_size("pix") * col_count)
    depth = ang_count * 2 * block

    half = col_count // HALVES
    outer, inner = phase_table(circle_pos, harmonics, ang_count, block)
    forward_high, forward_low = split_parts(real_table(outer, inner, False).reshape(2 * kept_count, depth))
    forward_table = lax.optimization_barrier(jnp.concatenate((forward_high, forward_low), 0))

    coefs = []
    for h in range(HALVES):
        send = jnp.transpose(grads[:, :, :, h * half:(h + 1) * half], (2, 0, 1, 3))
        moved = lax.all_to_all(send, ANG, split_axis=0, concat_axis=0, tiled=True)
        if h == 1:
            moved, backward_table = lax.optimization_barrier((moved, backward_table))
        stacked = jnp.dot(forward_table, moved.reshape(depth, half), preferred_element_type=jnp.float32)
        if h == 0:
            outer, inner, stacked = lax.optimization_barrier((outer, inner, stacked))
            backward_high, backward_low = split_parts(
                real_table(outer, inner, True).reshape(depth, 2 * kept_count)
            )
            backward_table = jnp.concatenate((backward_high, backward_low, backward_high), 1)
        coefs.append((stacked[: 2 * kept_count] + stacked[2 * kept_count:]) * (1.0 / math.sqrt(angle_count)))
    coef = jnp.concatenate(coefs, 1)
    coef_re = coef[:kept_count]
    coef_im = coef[kept_count:]
    square_sums = jnp.sum(weight[None, :] * (coef_re * coef_re + coef_im * coef_im), axis=1)
    harmonic_rms = jnp.sqrt(global_sum(square_sums) / cell_count + 1e-06)
    factor = weight[None, :] / harmonic_rms[:, None]
    step = coef * jnp.concatenate((factor, factor), 0)

    step_high, step_low = split_parts(step)
    step_stack = jnp.concatenate((step_high, step_high, step_low), 0)
    synthesis = jnp.dot(backward_table, step_stack, preferred_element_type=jnp.float32)
    update = (synthesis * (1.0 / math.sqrt(kept_count))).astype(jnp.bfloat16)
    update = update.reshape(ang_count, 2, block, col_count)
    back = lax.all_to_all(update, ANG, split_axis=0, concat_axis=0, tiled=True)
    back = jnp.transpose(back, (1, 2, 0, 3))
    return (back, harmonic_rms)


def solution(mesh):
    devices = mesh.devices.reshape(4, 2, 4, 2, mesh.shape["pix"])
    physical = Mesh(devices, ALL)
    placed = (P(None, ANG, "pix", None), P(), P(), P())
    return jax.shard_map(
        body,
        mesh=physical,
        in_specs=placed,
        out_specs=(P(None, ANG, "pix", None), P()),
        check_vma=False,
    )
```

```python
import math

import jax
import jax.numpy as jnp
from jax import lax
from jax.sharding import Mesh
from jax.sharding import PartitionSpec as P

ANG = ("x", "yl", "z", "c")
ALL = ANG + ("pix",)


def phase_pair(product, modulus):
    radians = (product % modulus).astype(jnp.float32) * (2.0 * math.pi / modulus)
    return (jnp.cos(radians), jnp.sin(radians))


def split_parts(value):
    if value.dtype == jnp.bfloat16:
        return (value,)
    high = value.astype(jnp.bfloat16)
    low = (value - high.astype(jnp.float32)).astype(jnp.bfloat16)
    return (high, low)


def split_dot(left, right, dims):
    left_parts = split_parts(left)
    right_parts = split_parts(right)
    total = None
    for left_rank, left_piece in enumerate(left_parts):
        for right_rank, right_piece in enumerate(right_parts):
            if left_rank + right_rank <= 1:
                term = lax.dot_general(
                    left_piece, right_piece, (dims, ((), ())), preferred_element_type=jnp.float32
                )
                total = term if total is None else total + term
    return total


def global_sum(value):
    for axis in (("c",), ("yl", "pix"), ("x",), ("z",)):
        size = lax.axis_size(axis)
        if size == 2:
            value = value + lax.ppermute(value, axis, [(0, 1), (1, 0)])
            continue
        parts = [value] + [
            lax.ppermute(value, axis, [(i, (i + shift) % size) for i in range(size)]) for shift in range(1, size)
        ]
        order = (lax.axis_index(axis) - jnp.arange(size)) % size
        ordered = jnp.stack(parts)[order]
        value = ordered[0]
        for position in range(1, size):
            value = value + ordered[position]
    return value


HALVES = 2


def phase_table(circle_pos, harmonics, ang_count, block):
    angle_count = circle_pos.shape[0]
    residues = circle_pos.reshape(ang_count, block)[:, 0]
    outer = phase_pair(harmonics[:, None] * residues[None, :], angle_count)
    steps = jnp.arange(block, dtype=jnp.int32)
    inner = phase_pair(harmonics[:, None] * steps[None, :], block)
    return (outer, inner)


def real_table(outer, inner, transposed):
    outer_cos, outer_sin = outer
    inner_cos, inner_sin = inner
    if transposed:
        outer_cos, outer_sin = outer_cos.T[:, None, None, :], outer_sin.T[:, None, None, :]
        inner_cos, inner_sin = inner_cos.T[None, None, :, :], inner_sin.T[None, None, :, :]
        axis_ri, axis_k = 1, 3
    else:
        outer_cos, outer_sin = outer_cos[:, :, None, None], outer_sin[:, :, None, None]
        inner_cos, inner_sin = inner_cos[:, None, None, :], inner_sin[:, None, None, :]
        axis_ri, axis_k = 2, 0
    phase_cos = outer_cos * inner_cos - outer_sin * inner_sin
    phase_sin = outer_sin * inner_cos + outer_cos * inner_sin
    return jnp.concatenate(
        (
            jnp.concatenate((phase_cos, phase_sin), axis_ri),
            jnp.concatenate((-phase_sin, phase_cos), axis_ri),
        ),
        axis_k,
    )


def body(grads, circle_pos, harmonics, support):
    ang_count = lax.axis_size(ANG)
    _, block, row_pix, col_count = grads.shape
    angle_count = circle_pos.shape[0]
    kept_count = harmonics.shape[0]
    row_start = lax.axis_index("pix") * row_pix + lax.axis_index(ANG)
    weight = lax.dynamic_slice_in_dim(support, row_start, 1, 0).astype(jnp.float32).reshape(-1)
    cell_count = float(row_pix * lax.axis_size("pix") * col_count)
    depth = ang_count * 2 * block

    half = col_count // HALVES
    outer, inner = phase_table(circle_pos, harmonics, ang_count, block)
    forward_high, forward_low = split_parts(real_table(outer, inner, False).reshape(2 * kept_count, depth))
    forward_table = lax.optimization_barrier(jnp.concatenate((forward_high, forward_low), 0))

    coefs = []
    for h in range(HALVES):
        send = jnp.transpose(grads[:, :, :, h * half:(h + 1) * half], (2, 0, 1, 3))
        moved = lax.all_to_all(send, ANG, split_axis=0, concat_axis=0, tiled=True)
        if h == 1:
            moved, backward_table = lax.optimization_barrier((moved, backward_table))
        stacked = jnp.dot(forward_table, moved.reshape(depth, half), preferred_element_type=jnp.float32)
        if h == 0:
            outer, inner, stacked = lax.optimization_barrier((outer, inner, stacked))
            backward_high, backward_low = split_parts(
                real_table(outer, inner, True).reshape(depth, 2 * kept_count)
            )
            backward_table = jnp.concatenate((backward_high, backward_low, backward_high), 1)
        coefs.append((stacked[: 2 * kept_count] + stacked[2 * kept_count:]) * (1.0 / math.sqrt(angle_count)))
    coef = jnp.concatenate(coefs, 1)
    coef_re = coef[:kept_count]
    coef_im = coef[kept_count:]
    square_sums = jnp.sum(weight[None, :] * (coef_re * coef_re + coef_im * coef_im), axis=1)
    harmonic_rms = jnp.sqrt(global_sum(square_sums) / cell_count + 1e-06)
    factor = weight[None, :] / harmonic_rms[:, None]
    step = coef * jnp.concatenate((factor, factor), 0)

    step_high, step_low = split_parts(step)
    step_stack = jnp.concatenate((step_high, step_high, step_low), 0)
    synthesis = jnp.dot(backward_table, step_stack, preferred_element_type=jnp.float32)
    update = (synthesis * (1.0 / math.sqrt(kept_count))).astype(jnp.bfloat16)
    update = update.reshape(ang_count, 2, block, col_count)
    back = lax.all_to_all(update, ANG, split_axis=0, concat_axis=0, tiled=True)
    back = jnp.transpose(back, (1, 2, 0, 3))
    return (back, harmonic_rms)


def solution(mesh):
    devices = mesh.devices.reshape(4, 2, 4, 2, mesh.shape["pix"])
    physical = Mesh(devices, ALL)
    placed = (P(None, ANG, "pix", None), P(), P(), P())
    return jax.shard_map(
        body,
        mesh=physical,
        in_specs=placed,
        out_specs=(P(None, ANG, "pix", None), P()),
        check_vma=False,
    )
```

```python
import math

import jax
import jax.numpy as jnp
from jax import lax
from jax.sharding import Mesh
from jax.sharding import PartitionSpec as P

ANG = ("x", "yl", "z", "c")
ALL = ANG + ("pix",)


def phase_pair(product, modulus):
    radians = (product % modulus).astype(jnp.float32) * (2.0 * math.pi / modulus)
    return (jnp.cos(radians), jnp.sin(radians))


def split_parts(value):
    if value.dtype == jnp.bfloat16:
        return (value,)
    high = value.astype(jnp.bfloat16)
    low = (value - high.astype(jnp.float32)).astype(jnp.bfloat16)
    return (high, low)


def split_dot(left, right, dims):
    left_parts = split_parts(left)
    right_parts = split_parts(right)
    total = None
    for left_rank, left_piece in enumerate(left_parts):
        for right_rank, right_piece in enumerate(right_parts):
            if left_rank + right_rank <= 1:
                term = lax.dot_general(
                    left_piece, right_piece, (dims, ((), ())), preferred_element_type=jnp.float32
                )
                total = term if total is None else total + term
    return total


def global_sum(value):
    for axis in ("c", "pix", "yl", "x", "z"):
        size = lax.axis_size(axis)
        if size == 2:
            value = value + lax.ppermute(value, axis, [(0, 1), (1, 0)])
            continue
        parts = [value] + [
            lax.ppermute(value, axis, [(i, (i + shift) % size) for i in range(size)]) for shift in range(1, size)
        ]
        order = (lax.axis_index(axis) - jnp.arange(size)) % size
        ordered = jnp.stack(parts)[order]
        value = ordered[0]
        for position in range(1, size):
            value = value + ordered[position]
    return value


HALVES = 2


def phase_table(circle_pos, harmonics, ang_count, block):
    angle_count = circle_pos.shape[0]
    residues = circle_pos.reshape(ang_count, block)[:, 0]
    outer = phase_pair(harmonics[:, None] * residues[None, :], angle_count)
    steps = jnp.arange(block, dtype=jnp.int32)
    inner = phase_pair(harmonics[:, None] * steps[None, :], block)
    return (outer, inner)


def real_table(outer, inner, transposed):
    outer_cos, outer_sin = outer
    inner_cos, inner_sin = inner
    if transposed:
        outer_cos, outer_sin = outer_cos.T[:, None, None, :], outer_sin.T[:, None, None, :]
        inner_cos, inner_sin = inner_cos.T[None, None, :, :], inner_sin.T[None, None, :, :]
        axis_ri, axis_k = 1, 3
    else:
        outer_cos, outer_sin = outer_cos[:, :, None, None], outer_sin[:, :, None, None]
        inner_cos, inner_sin = inner_cos[:, None, None, :], inner_sin[:, None, None, :]
        axis_ri, axis_k = 2, 0
    phase_cos = outer_cos * inner_cos - outer_sin * inner_sin
    phase_sin = outer_sin * inner_cos + outer_cos * inner_sin
    return jnp.concatenate(
        (
            jnp.concatenate((phase_cos, phase_sin), axis_ri),
            jnp.concatenate((-phase_sin, phase_cos), axis_ri),
        ),
        axis_k,
    )


def body(grads, circle_pos, harmonics, support):
    ang_count = lax.axis_size(ANG)
    _, block, row_pix, col_count = grads.shape
    angle_count = circle_pos.shape[0]
    kept_count = harmonics.shape[0]
    row_start = lax.axis_index("pix") * row_pix + lax.axis_index(ANG)
    weight = lax.dynamic_slice_in_dim(support, row_start, 1, 0).astype(jnp.float32).reshape(-1)
    cell_count = float(row_pix * lax.axis_size("pix") * col_count)
    depth = ang_count * 2 * block

    half = col_count // HALVES
    outer, inner = phase_table(circle_pos, harmonics, ang_count, block)
    forward_high, forward_low = split_parts(real_table(outer, inner, False).reshape(2 * kept_count, depth))
    forward_table = lax.optimization_barrier(jnp.concatenate((forward_high, forward_low), 0))

    coefs = []
    for h in range(HALVES):
        source = grads if h == 0 else lax.optimization_barrier(grads)
        send = jnp.transpose(source[:, :, :, h * half:(h + 1) * half], (2, 0, 1, 3))
        moved = lax.all_to_all(send, ANG, split_axis=0, concat_axis=0, tiled=True)
        if h == 1:
            moved, backward_table = lax.optimization_barrier((moved, backward_table))
        stacked = jnp.dot(forward_table, moved.reshape(depth, half), preferred_element_type=jnp.float32)
        if h == 0:
            outer, inner, stacked = lax.optimization_barrier((outer, inner, stacked))
            backward_high, backward_low = split_parts(
                real_table(outer, inner, True).reshape(depth, 2 * kept_count)
            )
            backward_table = jnp.concatenate((backward_high, backward_low, backward_high), 1)
        coefs.append((stacked[: 2 * kept_count] + stacked[2 * kept_count:]) * (1.0 / math.sqrt(angle_count)))
    coef = jnp.concatenate(coefs, 1)
    coef_re = coef[:kept_count]
    coef_im = coef[kept_count:]
    square_sums = jnp.sum(weight[None, :] * (coef_re * coef_re + coef_im * coef_im), axis=1)
    harmonic_rms = jnp.sqrt(global_sum(square_sums) / cell_count + 1e-06)
    factor = weight[None, :] / harmonic_rms[:, None]
    step = coef * jnp.concatenate((factor, factor), 0)

    step_high, step_low = split_parts(step)
    step_stack = jnp.concatenate((step_high, step_high, step_low), 0)
    synthesis = jnp.dot(backward_table, step_stack, preferred_element_type=jnp.float32)
    update = (synthesis * (1.0 / math.sqrt(kept_count))).astype(jnp.bfloat16)
    update = update.reshape(ang_count, 2, block, col_count)
    back = lax.all_to_all(update, ANG, split_axis=0, concat_axis=0, tiled=True)
    back = jnp.transpose(back, (1, 2, 0, 3))
    return (back, harmonic_rms)


def solution(mesh):
    devices = mesh.devices.reshape(4, 2, 4, 2, mesh.shape["pix"])
    physical = Mesh(devices, ALL)
    placed = (P(None, ANG, "pix", None), P(), P(), P())
    return jax.shard_map(
        body,
        mesh=physical,
        in_specs=placed,
        out_specs=(P(None, ANG, "pix", None), P()),
        check_vma=False,
    )
```

```python
import math

import jax
import jax.numpy as jnp
from jax import lax
from jax.sharding import Mesh
from jax.sharding import PartitionSpec as P

ANG = ("x", "yl", "z", "c")
ALL = ANG + ("pix",)


def phase_pair(product, modulus):
    radians = (product % modulus).astype(jnp.float32) * (2.0 * math.pi / modulus)
    return (jnp.cos(radians), jnp.sin(radians))


def split_parts(value):
    if value.dtype == jnp.bfloat16:
        return (value,)
    high = value.astype(jnp.bfloat16)
    low = (value - high.astype(jnp.float32)).astype(jnp.bfloat16)
    return (high, low)


def split_dot(left, right, dims):
    left_parts = split_parts(left)
    right_parts = split_parts(right)
    total = None
    for left_rank, left_piece in enumerate(left_parts):
        for right_rank, right_piece in enumerate(right_parts):
            if left_rank + right_rank <= 1:
                term = lax.dot_general(
                    left_piece, right_piece, (dims, ((), ())), preferred_element_type=jnp.float32
                )
                total = term if total is None else total + term
    return total


def global_sum(value):
    for axis in ("c", "pix", "yl", "x", "z"):
        size = lax.axis_size(axis)
        if size == 2:
            value = value + lax.ppermute(value, axis, [(0, 1), (1, 0)])
            continue
        parts = [value] + [
            lax.ppermute(value, axis, [(i, (i + shift) % size) for i in range(size)]) for shift in range(1, size)
        ]
        value = (parts[0] + parts[2]) + (parts[1] + parts[3])
    return value


HALVES = 2


def phase_table(circle_pos, harmonics, ang_count, block):
    angle_count = circle_pos.shape[0]
    residues = circle_pos.reshape(ang_count, block)[:, 0]
    outer = phase_pair(harmonics[:, None] * residues[None, :], angle_count)
    steps = jnp.arange(block, dtype=jnp.int32)
    inner = phase_pair(harmonics[:, None] * steps[None, :], block)
    return (outer, inner)


def real_table(outer, inner, transposed):
    outer_cos, outer_sin = outer
    inner_cos, inner_sin = inner
    if transposed:
        outer_cos, outer_sin = outer_cos.T[:, None, None, :], outer_sin.T[:, None, None, :]
        inner_cos, inner_sin = inner_cos.T[None, None, :, :], inner_sin.T[None, None, :, :]
        axis_ri, axis_k = 1, 3
    else:
        outer_cos, outer_sin = outer_cos[:, :, None, None], outer_sin[:, :, None, None]
        inner_cos, inner_sin = inner_cos[:, None, None, :], inner_sin[:, None, None, :]
        axis_ri, axis_k = 2, 0
    phase_cos = outer_cos * inner_cos - outer_sin * inner_sin
    phase_sin = outer_sin * inner_cos + outer_cos * inner_sin
    return jnp.concatenate(
        (
            jnp.concatenate((phase_cos, phase_sin), axis_ri),
            jnp.concatenate((-phase_sin, phase_cos), axis_ri),
        ),
        axis_k,
    )


def body(grads, circle_pos, harmonics, support):
    ang_count = lax.axis_size(ANG)
    _, block, row_pix, col_count = grads.shape
    angle_count = circle_pos.shape[0]
    kept_count = harmonics.shape[0]
    row_start = lax.axis_index("pix") * row_pix + lax.axis_index(ANG)
    weight = lax.dynamic_slice_in_dim(support, row_start, 1, 0).astype(jnp.float32).reshape(-1)
    cell_count = float(row_pix * lax.axis_size("pix") * col_count)
    depth = ang_count * 2 * block

    half = col_count // HALVES
    outer, inner = phase_table(circle_pos, harmonics, ang_count, block)
    forward_high, forward_low = split_parts(real_table(outer, inner, False).reshape(2 * kept_count, depth))
    forward_table = lax.optimization_barrier(jnp.concatenate((forward_high, forward_low), 0))

    coefs = []
    for h in range(HALVES):
        source = grads if h == 0 else lax.optimization_barrier(grads)
        send = jnp.transpose(source[:, :, :, h * half:(h + 1) * half], (2, 0, 1, 3))
        moved = lax.all_to_all(send, ANG, split_axis=0, concat_axis=0, tiled=True)
        if h == 1:
            moved, backward_table = lax.optimization_barrier((moved, backward_table))
        stacked = jnp.dot(forward_table, moved.reshape(depth, half), preferred_element_type=jnp.float32)
        if h == 0:
            outer, inner, stacked = lax.optimization_barrier((outer, inner, stacked))
            backward_high, backward_low = split_parts(
                real_table(outer, inner, True).reshape(depth, 2 * kept_count)
            )
            backward_table = jnp.concatenate((backward_high, backward_low, backward_high), 1)
        coefs.append((stacked[: 2 * kept_count] + stacked[2 * kept_count:]) * (1.0 / math.sqrt(angle_count)))
    coef = jnp.concatenate(coefs, 1)
    coef_re = coef[:kept_count]
    coef_im = coef[kept_count:]
    square_sums = jnp.sum(weight[None, :] * (coef_re * coef_re + coef_im * coef_im), axis=1)
    harmonic_rms = jnp.sqrt(global_sum(square_sums) / cell_count + 1e-06)
    factor = weight[None, :] / harmonic_rms[:, None]
    step = coef * jnp.concatenate((factor, factor), 0)

    step_high, step_low = split_parts(step)
    step_stack = jnp.concatenate((step_high, step_high, step_low), 0)
    synthesis = jnp.dot(backward_table, step_stack, preferred_element_type=jnp.float32)
    update = (synthesis * (1.0 / math.sqrt(kept_count))).astype(jnp.bfloat16)
    update = update.reshape(ang_count, 2, block, col_count)
    back = lax.all_to_all(update, ANG, split_axis=0, concat_axis=0, tiled=True)
    back = jnp.transpose(back, (1, 2, 0, 3))
    return (back, harmonic_rms)


def solution(mesh):
    devices = mesh.devices.reshape(4, 2, 4, 2, mesh.shape["pix"])
    physical = Mesh(devices, ALL)
    placed = (P(None, ANG, "pix", None), P(), P(), P())
    return jax.shard_map(
        body,
        mesh=physical,
        in_specs=placed,
        out_specs=(P(None, ANG, "pix", None), P()),
        check_vma=False,
    )
```

```python
import math

import jax
import jax.numpy as jnp
from jax import lax
from jax.sharding import Mesh
from jax.sharding import PartitionSpec as P

ANG = ("x", "yl", "z", "c")
ALL = ANG + ("pix",)


def phase_pair(product, modulus):
    radians = (product % modulus).astype(jnp.float32) * (2.0 * math.pi / modulus)
    return (jnp.cos(radians), jnp.sin(radians))


def split_parts(value):
    if value.dtype == jnp.bfloat16:
        return (value,)
    high = value.astype(jnp.bfloat16)
    low = (value - high.astype(jnp.float32)).astype(jnp.bfloat16)
    return (high, low)


def split_dot(left, right, dims):
    left_parts = split_parts(left)
    right_parts = split_parts(right)
    total = None
    for left_rank, left_piece in enumerate(left_parts):
        for right_rank, right_piece in enumerate(right_parts):
            if left_rank + right_rank <= 1:
                term = lax.dot_general(
                    left_piece, right_piece, (dims, ((), ())), preferred_element_type=jnp.float32
                )
                total = term if total is None else total + term
    return total


def global_sum(value):
    for axis in (("c",), ("yl", "pix"), ("x",), ("z",)):
        size = lax.axis_size(axis)
        if size == 2:
            value = value + lax.ppermute(value, axis, [(0, 1), (1, 0)])
            continue
        parts = [value] + [
            lax.ppermute(value, axis, [(i, (i + shift) % size) for i in range(size)]) for shift in range(1, size)
        ]
        value = (parts[0] + parts[2]) + (parts[1] + parts[3])
    return value


HALVES = 2


def phase_table(circle_pos, harmonics, ang_count, block):
    angle_count = circle_pos.shape[0]
    residues = circle_pos.reshape(ang_count, block)[:, 0]
    outer = phase_pair(harmonics[:, None] * residues[None, :], angle_count)
    steps = jnp.arange(block, dtype=jnp.int32)
    inner = phase_pair(harmonics[:, None] * steps[None, :], block)
    return (outer, inner)


def real_table(outer, inner, transposed):
    outer_cos, outer_sin = outer
    inner_cos, inner_sin = inner
    if transposed:
        outer_cos, outer_sin = outer_cos.T[:, None, None, :], outer_sin.T[:, None, None, :]
        inner_cos, inner_sin = inner_cos.T[None, None, :, :], inner_sin.T[None, None, :, :]
        axis_ri, axis_k = 1, 3
    else:
        outer_cos, outer_sin = outer_cos[:, :, None, None], outer_sin[:, :, None, None]
        inner_cos, inner_sin = inner_cos[:, None, None, :], inner_sin[:, None, None, :]
        axis_ri, axis_k = 2, 0
    phase_cos = outer_cos * inner_cos - outer_sin * inner_sin
    phase_sin = outer_sin * inner_cos + outer_cos * inner_sin
    return jnp.concatenate(
        (
            jnp.concatenate((phase_cos, phase_sin), axis_ri),
            jnp.concatenate((-phase_sin, phase_cos), axis_ri),
        ),
        axis_k,
    )


def body(grads, circle_pos, harmonics, support):
    ang_count = lax.axis_size(ANG)
    _, block, row_pix, col_count = grads.shape
    angle_count = circle_pos.shape[0]
    kept_count = harmonics.shape[0]
    row_start = lax.axis_index("pix") * row_pix + lax.axis_index(ANG)
    weight = lax.dynamic_slice_in_dim(support, row_start, 1, 0).astype(jnp.float32).reshape(-1)
    cell_count = float(row_pix * lax.axis_size("pix") * col_count)
    depth = ang_count * 2 * block

    half = col_count // HALVES
    outer, inner = phase_table(circle_pos, harmonics, ang_count, block)
    forward_high, forward_low = split_parts(real_table(outer, inner, False).reshape(2 * kept_count, depth))
    forward_table = lax.optimization_barrier(jnp.concatenate((forward_high, forward_low), 0))

    coefs = []
    for h in range(HALVES):
        source = grads if h == 0 else lax.optimization_barrier(grads)
        send = jnp.transpose(source[:, :, :, h * half:(h + 1) * half], (2, 0, 1, 3))
        moved = lax.all_to_all(send, ANG, split_axis=0, concat_axis=0, tiled=True)
        if h == 1:
            moved, backward_table = lax.optimization_barrier((moved, backward_table))
        stacked = jnp.dot(forward_table, moved.reshape(depth, half), preferred_element_type=jnp.float32)
        if h == 0:
            outer, inner, stacked = lax.optimization_barrier((outer, inner, stacked))
            backward_high, backward_low = split_parts(
                real_table(outer, inner, True).reshape(depth, 2 * kept_count)
            )
            backward_table = jnp.concatenate((backward_high, backward_low, backward_high), 1)
        coefs.append((stacked[: 2 * kept_count] + stacked[2 * kept_count:]) * (1.0 / math.sqrt(angle_count)))
    coef = jnp.concatenate(coefs, 1)
    coef_re = coef[:kept_count]
    coef_im = coef[kept_count:]
    square_sums = jnp.sum(weight[None, :] * (coef_re * coef_re + coef_im * coef_im), axis=1)
    harmonic_rms = jnp.sqrt(global_sum(square_sums) / cell_count + 1e-06)
    factor = weight[None, :] / harmonic_rms[:, None]
    step = coef * jnp.concatenate((factor, factor), 0)

    step_high, step_low = split_parts(step)
    step_stack = jnp.concatenate((step_high, step_high, step_low), 0)
    synthesis = jnp.dot(backward_table, step_stack, preferred_element_type=jnp.float32)
    update = (synthesis * (1.0 / math.sqrt(kept_count))).astype(jnp.bfloat16)
    update = update.reshape(ang_count, 2, block, col_count)
    back = lax.all_to_all(update, ANG, split_axis=0, concat_axis=0, tiled=True)
    back = jnp.transpose(back, (1, 2, 0, 3))
    return (back, harmonic_rms)


def solution(mesh):
    devices = mesh.devices.reshape(4, 2, 4, 2, mesh.shape["pix"])
    physical = Mesh(devices, ALL)
    placed = (P(None, ANG, "pix", None), P(), P(), P())
    return jax.shard_map(
        body,
        mesh=physical,
        in_specs=placed,
        out_specs=(P(None, ANG, "pix", None), P()),
        check_vma=False,
    )
```
